512 devices in a mesh: row: 16 (over z), col: 32 (over y, x, core).
Axes of the slice: x: 4, y: 4, z: 16, core: 2. Of those that a mesh axis runs over, the one named last changes fastest.
Arguments:
- inputs: bfloat16 [2048, 8192], P('col', 'row'), may hold values from -6 to 6
- gate_pre: bfloat16 [2048, 14784], P('row', 'col'), may hold values from -6 to 6
- up_pre: bfloat16 [2048, 14784], P('row', 'col'), may hold values from -6 to 6
- w_gate: bfloat16 [8192, 14784], P('row', 'col'), may hold values from -0.0625 to 0.0625
- w_up: bfloat16 [8192, 14784], P('row', 'col'), may hold values from -0.0625 to 0.0625
- w_down: bfloat16 [14784, 8192], P('col', 'row'), may hold values from -0.046875 to 0.046875
- grad_out: bfloat16 [2048, 8192], P('col', 'row'), may hold values from -1.5 to 1.5
Outputs:
- grad_in: bfloat16 [2048, 8192], P('col', 'row')
- grad_gate: bfloat16 [8192, 14784], P('row', 'col')
- grad_up: bfloat16 [8192, 14784], P('row', 'col')
- grad_down: bfloat16 [14784, 8192], P('col', 'row')
The draws below stay inside these ranges and needn't reach their ends.
All inputs are finite; a program needn't handle non-finite values.
Results may differ from the reference program's by a relative error of at most 0.025.
Values may be sent and summed in bfloat16 or wider, within the bound.
No kernel may reach another device: no remote copies, remote signals or barrier semaphores. Data moves between devices by JAX's collectives and lax.ppermute only.
A program may use at most 64 MiB of HBM per device.

```python
import jax
import jax.numpy as jnp
from jax import lax

D = 8192
FF = 14784
TOKENS = 2048
N_ROW = 16
N_COL = 32


def spiked(values, stream_key, source, target, blocks, factor):
    owner, partner = [(jnp.arange(values.shape[dim]) // (values.shape[dim] // blocks)).reshape([-1 if axis == dim else 1 for axis in range(values.ndim)]) for dim in (source, target)]
    chosen = jax.random.permutation(stream_key, blocks)[partner]
    strong = (owner == chosen) | (owner == (partner + blocks // 2) % blocks)
    return jnp.where(strong, factor * values, values)


def steps_of(key, dims, shards, least, high):
    def one(position, blocks):
        steps = jax.random.uniform(jax.random.fold_in(jax.random.fold_in(key, 6), position), (blocks,), jnp.float32, least / len(shards), high / len(shards))
        return jnp.repeat(jnp.exp(steps), dims[position] // blocks).reshape((-1,) + (1,) * (len(dims) - position - 1))

    factor_of = one(*shards[0])
    for cut in shards[1:]:
        factor_of = factor_of * one(*cut)
    return factor_of


def centred(rng, shape, deviation, limit, shards=(), kind=jnp.bfloat16):
    factor_of = steps_of(rng, shape, shards, -0.22, 0.18) if shards else 1.0
    drawn = jax.random.normal(rng, shape, jnp.float32) * deviation * factor_of
    return jnp.minimum(jnp.maximum(drawn, -limit), limit).astype(kind)


def noise_with(stream_key, extent, scale, bound, shards, heavy, kind=jnp.bfloat16):
    array = scale * jax.random.normal(stream_key, extent, jnp.float32)
    if shards:
        array = array * steps_of(stream_key, extent, shards, -0.22, 0.18)
    return jnp.clip(spiked(array, jax.random.fold_in(stream_key, 3), *heavy), -bound, bound).astype(kind)


def setup_inputs(seed: int = 0) -> dict:
    key_list = jax.random.split(jax.random.key(seed), 8)
    inputs = centred(key_list[0], (TOKENS, D), 1.0, 6.0, ((0, 32), (1, 16)))
    gate_pre = centred(key_list[1], (TOKENS, FF), 1.0, 6.0, ((0, 16), (1, 32)))
    up_pre = noise_with(key_list[2], (TOKENS, FF), 1.0, 6.0, ((0, 16), (1, 32)), (1, 0, 32, 2.75))
    w_gate = centred(key_list[3], (D, FF), D ** -0.5, 0.0625, ((0, 16), (1, 32)))
    w_up = centred(key_list[4], (D, FF), D ** -0.5, 0.0625, ((0, 16), (1, 32)))
    w_down = centred(key_list[5], (FF, D), FF ** -0.5, 0.046875, ((0, 32), (1, 16)))
    grad_out = noise_with(key_list[6], (TOKENS, D), 0.25, 1.5, ((0, 32), (1, 16)), (1, 0, 32, 2.75))
    return {"inputs": inputs, "gate_pre": gate_pre, "up_pre": up_pre, "w_gate": w_gate, "w_up": w_up, "w_down": w_down, "grad_out": grad_out}


def contract_rows(left, right):
    return lax.dot_general(left, right, (((0,), (0,)), ((), ())), preferred_element_type=jnp.float32)


def contract_cols(left, right):
    return lax.dot_general(left, right, (((1,), (1,)), ((), ())), preferred_element_type=jnp.float32)


def pointwise(gate_pre, up_pre, hidden_grad):
    gate_value = gate_pre.astype(jnp.float32)
    up_value = up_pre.astype(jnp.float32)
    sigmoid_gate = jax.nn.sigmoid(gate_value)
    activated = gate_value * sigmoid_gate
    hidden = (activated * up_value).astype(jnp.bfloat16)
    up_grad = (hidden_grad * activated).astype(jnp.bfloat16)
    gate_grad = (hidden_grad * up_value * sigmoid_gate * (1.0 + gate_value * (1.0 - sigmoid_gate))).astype(jnp.bfloat16)
    return hidden, gate_grad, up_grad


def reference(inputs, gate_pre, up_pre, w_gate, w_up, w_down, grad_out):
    width_block = D // N_ROW
    hidden_block = FF // N_COL

    def add_hidden(block_index, total):
        offset = (block_index * width_block).astype(jnp.int32)
        rows_out = lax.dynamic_slice_in_dim(grad_out, offset, width_block, 1)
        rows_down = lax.dynamic_slice_in_dim(w_down, offset, width_block, 1)
        term = lax.optimization_barrier(contract_cols(rows_out, rows_down).astype(jnp.bfloat16))
        return total + term.astype(jnp.float32)

    hidden_grad = lax.fori_loop(0, N_ROW, add_hidden, jnp.zeros((TOKENS, FF), jnp.float32))
    hidden, gate_grad, up_grad = pointwise(gate_pre, up_pre, hidden_grad)
    grad_down = contract_rows(hidden, grad_out).astype(jnp.bfloat16)
    grad_gate = contract_rows(inputs, gate_grad).astype(jnp.bfloat16)
    grad_up = contract_rows(inputs, up_grad).astype(jnp.bfloat16)

    def add_input(block_index, total):
        offset = (block_index * hidden_block).astype(jnp.int32)
        cols_gate = lax.dynamic_slice_in_dim(gate_grad, offset, hidden_block, 1)
        cols_up = lax.dynamic_slice_in_dim(up_grad, offset, hidden_block, 1)
        weight_gate = lax.dynamic_slice_in_dim(w_gate, offset, hidden_block, 1)
        weight_up = lax.dynamic_slice_in_dim(w_up, offset, hidden_block, 1)
        term = contract_cols(cols_gate, weight_gate) + contract_cols(cols_up, weight_up)
        term = lax.optimization_barrier(term.astype(jnp.bfloat16))
        return total + term.astype(jnp.float32)

    grad_in = lax.fori_loop(0, N_COL, add_input, jnp.zeros((TOKENS, D), jnp.float32)).astype(jnp.bfloat16)
    return (grad_in, grad_gate, grad_up, grad_down)
```

```python
import jax
import jax.numpy as jnp
from jax import lax
from jax.sharding import PartitionSpec as P


def contract_rows(left, right):
    return lax.dot_general(
        left, right, (((0,), (0,)), ((), ())), preferred_element_type=jnp.float32
    )


def contract_cols(left, right):
    return lax.dot_general(
        left, right, (((1,), (1,)), ((), ())), preferred_element_type=jnp.float32
    )


def pointwise(gate_pre, up_pre, hidden_grad):
    gate_value = gate_pre.astype(jnp.float32)
    up_value = up_pre.astype(jnp.float32)
    sigmoid_gate = jax.nn.sigmoid(gate_value)
    activated = gate_value * sigmoid_gate
    hidden = (activated * up_value).astype(jnp.bfloat16)
    up_grad = (hidden_grad * activated).astype(jnp.bfloat16)
    gate_grad = (
        hidden_grad * up_value * sigmoid_gate * (1.0 + gate_value * (1.0 - sigmoid_gate))
    ).astype(jnp.bfloat16)
    return (hidden, gate_grad, up_grad)


def _shifts(n):
    up = [(j, (j + 1) % n) for j in range(n)]
    down = [(j, (j - 1) % n) for j in range(n)]
    return up, down


def ring_all_gather(x, axis, n):
    me = lax.axis_index(axis)
    up, down = _shifts(n)
    n_up = n // 2
    n_down = n - 1 - n_up
    out = jnp.zeros((n,) + x.shape, x.dtype)
    out = lax.dynamic_update_index_in_dim(out, x, me, 0)
    a = x
    b = x
    for s in range(1, n_up + 1):
        a = lax.ppermute(a, axis, up)
        out = lax.dynamic_update_index_in_dim(out, a, (me - s + n) % n, 0)
        if s <= n_down:
            b = lax.ppermute(b, axis, down)
            out = lax.dynamic_update_index_in_dim(out, b, (me + s) % n, 0)
    return out


def ring_reduce_scatter(parts, axis, n, wire_dtype):
    me = lax.axis_index(axis)
    up, down = _shifts(n)
    n_up = n // 2
    n_down = n - 1 - n_up

    def block(j):
        return lax.dynamic_index_in_dim(parts, (j + 2 * n) % n, 0, keepdims=False).astype(
            jnp.float32
        )

    a = block(me + n_up)
    b = block(me - n_down)
    for s in range(n_up):
        a = lax.ppermute(a.astype(wire_dtype), axis, up).astype(jnp.float32)
        if s < n_up - 1:
            a = a + block(me + n_up - 1 - s)
        if s < n_down:
            b = lax.ppermute(b.astype(wire_dtype), axis, down).astype(jnp.float32)
            if s < n_down - 1:
                b = b + block(me - n_down + 1 + s)
    return block(me) + a + b


def shards(inputs, gate_pre, up_pre, w_gate, w_up, w_down, grad_out, n_row):
    tokens_row, hidden_units = gate_pre.shape
    pre = jnp.stack([gate_pre, up_pre], axis=1)
    all_pre = ring_all_gather(pre, "row", n_row).reshape(
        (n_row * tokens_row, 2, hidden_units)
    )
    all_grad_out = lax.all_gather(grad_out, "col", axis=0, tiled=True)
    all_inputs = lax.all_gather(inputs, "col", axis=0, tiled=True)
    part = contract_cols(all_grad_out, w_down).astype(jnp.bfloat16)
    part = part.reshape((n_row, tokens_row, hidden_units))
    own = ring_reduce_scatter(part, "row", n_row, jnp.bfloat16).astype(jnp.bfloat16)
    hidden_grad = ring_all_gather(own, "row", n_row).reshape(
        (n_row * tokens_row, hidden_units)
    )
    hidden, gate_grad, up_grad = pointwise(
        all_pre[:, 0], all_pre[:, 1], hidden_grad.astype(jnp.float32)
    )
    grad_down = contract_rows(hidden, all_grad_out).astype(jnp.bfloat16)
    grad_gate = contract_rows(all_inputs, gate_grad).astype(jnp.bfloat16)
    grad_up = contract_rows(all_inputs, up_grad).astype(jnp.bfloat16)
    grad_in = lax.psum_scatter(
        (contract_cols(gate_grad, w_gate) + contract_cols(up_grad, w_up)).astype(jnp.bfloat16),
        "col",
        scatter_dimension=0,
        tiled=True,
    )
    return (grad_in, grad_gate, grad_up, grad_down)


def solution(mesh):
    n_row = mesh.shape["row"]

    def body(*args):
        return shards(*args, n_row=n_row)

    return jax.shard_map(
        body,
        mesh=mesh,
        in_specs=(
            P("col", "row"),
            P("row", "col"),
            P("row", "col"),
            P("row", "col"),
            P("row", "col"),
            P("col", "row"),
            P("col", "row"),
        ),
        out_specs=(P("col", "row"), P("row", "col"), P("row", "col"), P("col", "row")),
        check_vma=False,
    )
```

```python
import jax
import jax.numpy as jnp
from jax import lax
from jax.sharding import PartitionSpec as P


def contract_rows(left, right):
    return lax.dot_general(
        left, right, (((0,), (0,)), ((), ())), preferred_element_type=jnp.float32
    )


def contract_cols(left, right):
    return lax.dot_general(
        left, right, (((1,), (1,)), ((), ())), preferred_element_type=jnp.float32
    )


def pointwise(gate_pre, up_pre, hidden_grad):
    gate_value = gate_pre.astype(jnp.float32)
    up_value = up_pre.astype(jnp.float32)
    sigmoid_gate = jax.nn.sigmoid(gate_value)
    activated = gate_value * sigmoid_gate
    hidden = (activated * up_value).astype(jnp.bfloat16)
    up_grad = (hidden_grad * activated).astype(jnp.bfloat16)
    gate_grad = (
        hidden_grad * up_value * sigmoid_gate * (1.0 + gate_value * (1.0 - sigmoid_gate))
    ).astype(jnp.bfloat16)
    return (hidden, gate_grad, up_grad)


def _shifts(n):
    up = [(j, (j + 1) % n) for j in range(n)]
    down = [(j, (j - 1) % n) for j in range(n)]
    return up, down


def ring_all_gather(x, axis, n):
    me = lax.axis_index(axis)
    up, down = _shifts(n)
    n_up = n // 2
    n_down = n - 1 - n_up
    held = {0: x}
    a = x
    b = x
    for s in range(1, n_up + 1):
        a = lax.ppermute(a, axis, up)
        held[-s] = a
        if s <= n_down:
            b = lax.ppermute(b, axis, down)
            held[s] = b
    ring_order = jnp.stack([held[d] for d in range(-n_up, n_down + 1)])
    return jnp.take(ring_order, (jnp.arange(n) - me + n_up) % n, axis=0)


def ring_reduce_scatter(parts, axis, n, wire_dtype):
    me = lax.axis_index(axis)
    up, down = _shifts(n)
    n_up = n // 2
    n_down = n - 1 - n_up

    def block(j):
        return lax.dynamic_index_in_dim(parts, (j + 2 * n) % n, 0, keepdims=False).astype(
            jnp.float32
        )

    a = block(me + n_up)
    b = block(me - n_down)
    for s in range(n_up):
        a = lax.ppermute(a.astype(wire_dtype), axis, up).astype(jnp.float32)
        if s < n_up - 1:
            a = a + block(me + n_up - 1 - s)
        if s < n_down:
            b = lax.ppermute(b.astype(wire_dtype), axis, down).astype(jnp.float32)
            if s < n_down - 1:
                b = b + block(me - n_down + 1 + s)
    return block(me) + a + b


def shards(inputs, gate_pre, up_pre, w_gate, w_up, w_down, grad_out, n_row):
    tokens_row, hidden_units = gate_pre.shape
    all_grad_out = lax.all_gather(grad_out, "col", axis=0, tiled=True)
    all_inputs = lax.all_gather(inputs, "col", axis=0, tiled=True)
    part = contract_cols(all_grad_out, w_down).astype(jnp.bfloat16)
    part = part.reshape((n_row, tokens_row, hidden_units))
    own_grad = ring_reduce_scatter(part, "row", n_row, jnp.bfloat16)
    own = jnp.stack(pointwise(gate_pre, up_pre, own_grad), axis=1)
    gathered = ring_all_gather(own, "row", n_row).reshape(
        (n_row * tokens_row, 3, hidden_units)
    )
    hidden, gate_grad, up_grad = gathered[:, 0], gathered[:, 1], gathered[:, 2]
    grad_down = contract_rows(hidden, all_grad_out).astype(jnp.bfloat16)
    grad_gate = contract_rows(all_inputs, gate_grad).astype(jnp.bfloat16)
    grad_up = contract_rows(all_inputs, up_grad).astype(jnp.bfloat16)
    grad_in = lax.psum_scatter(
        (contract_cols(gate_grad, w_gate) + contract_cols(up_grad, w_up)).astype(jnp.bfloat16),
        "col",
        scatter_dimension=0,
        tiled=True,
    )
    return (grad_in, grad_gate, grad_up, grad_down)


def solution(mesh):
    n_row = mesh.shape["row"]

    def body(*args):
        return shards(*args, n_row=n_row)

    return jax.shard_map(
        body,
        mesh=mesh,
        in_specs=(
            P("col", "row"),
            P("row", "col"),
            P("row", "col"),
            P("row", "col"),
            P("row", "col"),
            P("col", "row"),
            P("col", "row"),
        ),
        out_specs=(P("col", "row"), P("row", "col"), P("row", "col"), P("col", "row")),
        check_vma=False,
    )
```

```python
import jax
import jax.numpy as jnp
from jax import lax
from jax.sharding import PartitionSpec as P


def contract_rows(left, right):
    return lax.dot_general(
        left, right, (((0,), (0,)), ((), ())), preferred_element_type=jnp.float32
    )


def contract_cols(left, right):
    return lax.dot_general(
        left, right, (((1,), (1,)), ((), ())), preferred_element_type=jnp.float32
    )


def pointwise(gate_pre, up_pre, hidden_grad):
    gate_value = gate_pre.astype(jnp.float32)
    up_value = up_pre.astype(jnp.float32)
    sigmoid_gate = jax.nn.sigmoid(gate_value)
    activated = gate_value * sigmoid_gate
    hidden = (activated * up_value).astype(jnp.bfloat16)
    up_grad = (hidden_grad * activated).astype(jnp.bfloat16)
    gate_grad = (
        hidden_grad * up_value * sigmoid_gate * (1.0 + gate_value * (1.0 - sigmoid_gate))
    ).astype(jnp.bfloat16)
    return (hidden, gate_grad, up_grad)


def _shifts(n):
    up = [(j, (j + 1) % n) for j in range(n)]
    down = [(j, (j - 1) % n) for j in range(n)]
    return up, down


def ring_all_gather(x, axis, n):
    me = lax.axis_index(axis)
    up, down = _shifts(n)
    n_up = n // 2
    n_down = n - 1 - n_up
    held = {0: x}
    a = x
    b = x
    for s in range(1, n_up + 1):
        a = lax.ppermute(a, axis, up)
        held[-s] = a
        if s <= n_down:
            b = lax.ppermute(b, axis, down)
            held[s] = b
    ring_order = jnp.stack([held[d] for d in range(-n_up, n_down + 1)], axis=1)
    return jnp.take(ring_order, (jnp.arange(n) - me + n_up) % n, axis=1)


def ring_reduce_scatter(parts, axis, n, wire_dtype, me=None, up=None, down=None):
    if me is None:
        me = lax.axis_index(axis)
        up, down = _shifts(n)
    n_up = n // 2
    n_down = n - 1 - n_up

    def block(j):
        return lax.dynamic_index_in_dim(parts, (j + 2 * n) % n, 0, keepdims=False).astype(
            jnp.float32
        )

    a = block(me + n_up)
    b = block(me - n_down)
    for s in range(n_up):
        a = lax.ppermute(a.astype(wire_dtype), axis, up).astype(jnp.float32)
        if s < n_up - 1:
            a = a + block(me + n_up - 1 - s)
        if s < n_down:
            b = lax.ppermute(b.astype(wire_dtype), axis, down).astype(jnp.float32)
            if s < n_down - 1:
                b = b + block(me - n_down + 1 + s)
    return block(me) + a + b


def col_reduce_scatter(blocks, n_x, n_y):
    n_col = 2 * n_x * n_y
    c = lax.axis_index("col")
    core = c % 2
    x = (c // 2) % n_x
    y = c // (2 * n_x)
    m = blocks.shape[1] // 2
    halves = blocks.reshape((n_y * n_x, 2, m) + blocks.shape[2:]).astype(jnp.float32)
    keep = lax.dynamic_index_in_dim(halves, core, 1, keepdims=False)
    give = lax.dynamic_index_in_dim(halves, 1 - core, 1, keepdims=False)
    pair = [(j, j ^ 1) for j in range(n_col)]
    summed = keep + lax.ppermute(give, "col", pair)

    def idx(yy, xx, cc):
        return (yy * n_x + xx) * 2 + cc

    def ring(step, size, coord):
        pairs = []
        for yy in range(n_y):
            for xx in range(n_x):
                for cc in range(2):
                    if coord == "x":
                        pairs.append((idx(yy, xx, cc), idx(yy, (xx + step) % size, cc)))
                    else:
                        pairs.append((idx(yy, xx, cc), idx((yy + step) % size, xx, cc)))
        return pairs

    by_x = jnp.swapaxes(summed.reshape((n_y, n_x, m) + blocks.shape[2:]), 0, 1)
    over_x = ring_reduce_scatter(
        by_x, "col", n_x, jnp.bfloat16, me=x, up=ring(1, n_x, "x"), down=ring(-1, n_x, "x")
    )
    return ring_reduce_scatter(
        over_x, "col", n_y, jnp.bfloat16, me=y, up=ring(1, n_y, "y"), down=ring(-1, n_y, "y")
    )


def shards(inputs, gate_pre, up_pre, w_gate, w_up, w_down, grad_out, n_row, n_x, n_y):
    tokens_row, hidden_units = gate_pre.shape
    all_grad_out = lax.all_gather(grad_out, "col", axis=0, tiled=True)
    all_inputs = lax.all_gather(inputs, "col", axis=0, tiled=True)
    part = contract_cols(all_grad_out, w_down).astype(jnp.bfloat16)
    part = part.reshape((n_row, tokens_row, hidden_units))
    own_grad = ring_reduce_scatter(part, "row", n_row, jnp.bfloat16)
    own = jnp.stack(pointwise(gate_pre, up_pre, own_grad), axis=0)
    gathered = ring_all_gather(own, "row", n_row).reshape(
        (3, n_row * tokens_row, hidden_units)
    )
    hidden, gate_grad, up_grad = gathered[0], gathered[1], gathered[2]
    grad_down = contract_rows(hidden, all_grad_out).astype(jnp.bfloat16)
    grad_gate = contract_rows(all_inputs, gate_grad).astype(jnp.bfloat16)
    grad_up = contract_rows(all_inputs, up_grad).astype(jnp.bfloat16)
    grad_in_terms = (
        contract_cols(gate_grad, w_gate) + contract_cols(up_grad, w_up)
    ).astype(jnp.bfloat16)
    grad_in_terms = grad_in_terms.reshape((n_y * n_x, -1, grad_in_terms.shape[1]))
    grad_in = col_reduce_scatter(grad_in_terms, n_x, n_y).astype(jnp.bfloat16)
    return (grad_in, grad_gate, grad_up, grad_down)


def solution(mesh):
    n_row = mesh.shape["row"]
    try:
        n_x = len({d.coords[0] for d in mesh.devices.flat})
    except AttributeError:
        n_x = int(round((mesh.shape["col"] // 2) ** 0.5))
    n_y = mesh.shape["col"] // (2 * n_x)

    def body(*args):
        return shards(*args, n_row=n_row, n_x=n_x, n_y=n_y)

    return jax.shard_map(
        body,
        mesh=mesh,
        in_specs=(
            P("col", "row"),
            P("row", "col"),
            P("row", "col"),
            P("row", "col"),
            P("row", "col"),
            P("col", "row"),
            P("col", "row"),
        ),
        out_specs=(P("col", "row"), P("row", "col"), P("row", "col"), P("col", "row")),
        check_vma=False,
    )
```

```python
import jax
import jax.numpy as jnp
from jax import lax
from jax.sharding import PartitionSpec as P


def contract_rows(left, right):
    return lax.dot_general(
        left, right, (((0,), (0,)), ((), ())), preferred_element_type=jnp.float32
    )


def contract_cols(left, right):
    return lax.dot_general(
        left, right, (((1,), (1,)), ((), ())), preferred_element_type=jnp.float32
    )


def pointwise(gate_pre, up_pre, hidden_grad):
    gate_value = gate_pre.astype(jnp.float32)
    up_value = up_pre.astype(jnp.float32)
    sigmoid_gate = jax.nn.sigmoid(gate_value)
    activated = gate_value * sigmoid_gate
    hidden = (activated * up_value).astype(jnp.bfloat16)
    up_grad = (hidden_grad * activated).astype(jnp.bfloat16)
    gate_grad = (
        hidden_grad * up_value * sigmoid_gate * (1.0 + gate_value * (1.0 - sigmoid_gate))
    ).astype(jnp.bfloat16)
    return (hidden, gate_grad, up_grad)


def _shifts(n):
    up = [(j, (j + 1) % n) for j in range(n)]
    down = [(j, (j - 1) % n) for j in range(n)]
    return up, down


def ring_all_gather(x, axis, n):
    me = lax.axis_index(axis)
    up, down = _shifts(n)
    n_up = n // 2
    n_down = n - 1 - n_up
    held = {0: x}
    a = x
    b = x
    for s in range(1, n_up + 1):
        a = lax.ppermute(a, axis, up)
        held[-s] = a
        if s <= n_down:
            b = lax.ppermute(b, axis, down)
            held[s] = b
    ring_order = jnp.stack([held[d] for d in range(-n_up, n_down + 1)], axis=1)
    return jnp.take(ring_order, (jnp.arange(n) - me + n_up) % n, axis=1)


def ring_reduce_scatter(parts, axis, n, wire_dtype, me=None, up=None, down=None):
    if me is None:
        me = lax.axis_index(axis)
        up, down = _shifts(n)
    n_up = n // 2
    n_down = n - 1 - n_up

    def block(j):
        return lax.dynamic_index_in_dim(parts, (j + 2 * n) % n, 0, keepdims=False).astype(
            jnp.float32
        )

    a = block(me + n_up)
    b = block(me - n_down)
    for s in range(n_up):
        a = lax.ppermute(a.astype(wire_dtype), axis, up).astype(jnp.float32)
        if s < n_up - 1:
            a = a + block(me + n_up - 1 - s)
        if s < n_down:
            b = lax.ppermute(b.astype(wire_dtype), axis, down).astype(jnp.float32)
            if s < n_down - 1:
                b = b + block(me - n_down + 1 + s)
    return block(me) + a + b


def col_reduce_scatter(blocks, n_x, n_y):
    n_col = 2 * n_x * n_y
    c = lax.axis_index("col")
    core = c % 2
    x = (c // 2) % n_x
    y = c // (2 * n_x)
    m = blocks.shape[1] // 2
    halves = blocks.reshape((n_y * n_x, 2, m) + blocks.shape[2:]).astype(jnp.float32)
    keep = lax.dynamic_index_in_dim(halves, core, 1, keepdims=False)
    give = lax.dynamic_index_in_dim(halves, 1 - core, 1, keepdims=False)
    pair = [(j, j ^ 1) for j in range(n_col)]
    summed = keep + lax.ppermute(give, "col", pair)

    def idx(yy, xx, cc):
        return (yy * n_x + xx) * 2 + cc

    def ring(step, size, coord):
        pairs = []
        for yy in range(n_y):
            for xx in range(n_x):
                for cc in range(2):
                    if coord == "x":
                        pairs.append((idx(yy, xx, cc), idx(yy, (xx + step) % size, cc)))
                    else:
                        pairs.append((idx(yy, xx, cc), idx((yy + step) % size, xx, cc)))
        return pairs

    by_x = jnp.swapaxes(summed.reshape((n_y, n_x, m) + blocks.shape[2:]), 0, 1)
    over_x = ring_reduce_scatter(
        by_x, "col", n_x, jnp.bfloat16, me=x, up=ring(1, n_x, "x"), down=ring(-1, n_x, "x")
    )
    return ring_reduce_scatter(
        over_x, "col", n_y, jnp.bfloat16, me=y, up=ring(1, n_y, "y"), down=ring(-1, n_y, "y")
    )


def shards(inputs, gate_pre, up_pre, w_gate, w_up, w_down, grad_out, n_row, n_col):
    tokens_row, hidden_units = gate_pre.shape
    tokens_col, width = grad_out.shape
    spread = jnp.broadcast_to(grad_out[None], (n_col, tokens_col, width))
    all_grad_out = lax.all_to_all(spread, "col", 0, 0).reshape((n_col * tokens_col, width))
    all_inputs = lax.all_gather(inputs, "col", axis=0, tiled=True)
    part = contract_cols(all_grad_out, w_down).astype(jnp.bfloat16)
    part = part.reshape((n_row, tokens_row, hidden_units))
    own_grad = ring_reduce_scatter(part, "row", n_row, jnp.bfloat16)
    own = jnp.stack(pointwise(gate_pre, up_pre, own_grad), axis=0)

    me = lax.axis_index("row")
    up, down = _shifts(n_row)
    n_up = n_row // 2
    n_down = n_row - 1 - n_up
    sums = [None, None, None]
    terms = {}

    def use(block, offset):
        k = (me + offset + n_row) % n_row
        rows_out = lax.dynamic_slice_in_dim(all_grad_out, k * tokens_row, tokens_row, 0)
        rows_in = lax.dynamic_slice_in_dim(all_inputs, k * tokens_row, tokens_row, 0)
        hidden, gate_grad, up_grad = block[0], block[1], block[2]
        new = (
            contract_rows(hidden, rows_out),
            contract_rows(rows_in, gate_grad),
            contract_rows(rows_in, up_grad),
        )
        for i in range(3):
            sums[i] = new[i] if sums[i] is None else sums[i] + new[i]
        terms[offset] = (
            contract_cols(gate_grad, w_gate) + contract_cols(up_grad, w_up)
        ).astype(jnp.bfloat16)

    a = own
    b = own
    use(own, 0)
    for s in range(1, n_up + 1):
        a = lax.ppermute(a, "row", up)
        if s <= n_down:
            b = lax.ppermute(b, "row", down)
        use(a, -s)
        if s <= n_down:
            use(b, s)
    grad_down, grad_gate, grad_up = (v.astype(jnp.bfloat16) for v in sums)
    ring_order = jnp.stack([terms[d] for d in range(-n_up, n_down + 1)])
    natural = jnp.take(ring_order, (jnp.arange(n_row) - me + n_up) % n_row, axis=0)
    natural = natural.reshape((n_col, -1, width))
    received = lax.all_to_all(natural, "col", 0, 0)
    grad_in = received.astype(jnp.float32).sum(axis=0).astype(jnp.bfloat16)
    return (grad_in, grad_gate, grad_up, grad_down)


def solution(mesh):
    n_row = mesh.shape["row"]
    n_col = mesh.shape["col"]

    def body(*args):
        return shards(*args, n_row=n_row, n_col=n_col)

    return jax.shard_map(
        body,
        mesh=mesh,
        in_specs=(
            P("col", "row"),
            P("row", "col"),
            P("row", "col"),
            P("row", "col"),
            P("row", "col"),
            P("col", "row"),
            P("col", "row"),
        ),
        out_specs=(P("col", "row"), P("row", "col"), P("row", "col"), P("col", "row")),
        check_vma=False,
    )
```

```python
import jax
import jax.numpy as jnp
from jax import lax
from jax.sharding import PartitionSpec as P


def contract_rows(left, right):
    return lax.dot_general(
        left, right, (((0,), (0,)), ((), ())), preferred_element_type=jnp.float32
    )


def contract_cols(left, right):
    return lax.dot_general(
        left, right, (((1,), (1,)), ((), ())), preferred_element_type=jnp.float32
    )


def pointwise(gate_pre, up_pre, hidden_grad):
    gate_value = gate_pre.astype(jnp.float32)
    up_value = up_pre.astype(jnp.float32)
    sigmoid_gate = jax.nn.sigmoid(gate_value)
    activated = gate_value * sigmoid_gate
    hidden = (activated * up_value).astype(jnp.bfloat16)
    up_grad = (hidden_grad * activated).astype(jnp.bfloat16)
    gate_grad = (
        hidden_grad * up_value * sigmoid_gate * (1.0 + gate_value * (1.0 - sigmoid_gate))
    ).astype(jnp.bfloat16)
    return (hidden, gate_grad, up_grad)


def _shifts(n):
    up = [(j, (j + 1) % n) for j in range(n)]
    down = [(j, (j - 1) % n) for j in range(n)]
    return up, down


def ring_all_gather(x, axis, n):
    me = lax.axis_index(axis)
    up, down = _shifts(n)
    n_up = n // 2
    n_down = n - 1 - n_up
    held = {0: x}
    a = x
    b = x
    for s in range(1, n_up + 1):
        a = lax.ppermute(a, axis, up)
        held[-s] = a
        if s <= n_down:
            b = lax.ppermute(b, axis, down)
            held[s] = b
    ring_order = jnp.stack([held[d] for d in range(-n_up, n_down + 1)], axis=1)
    return jnp.take(ring_order, (jnp.arange(n) - me + n_up) % n, axis=1)


def ring_reduce_scatter(parts, axis, n, wire_dtype, me=None, up=None, down=None):
    if me is None:
        me = lax.axis_index(axis)
        up, down = _shifts(n)
    n_up = n // 2
    n_down = n - 1 - n_up

    def block(j):
        return lax.dynamic_index_in_dim(parts, (j + 2 * n) % n, 0, keepdims=False).astype(
            jnp.float32
        )

    a = block(me + n_up)
    b = block(me - n_down)
    for s in range(n_up):
        a = lax.ppermute(a.astype(wire_dtype), axis, up).astype(jnp.float32)
        if s < n_up - 1:
            a = a + block(me + n_up - 1 - s)
        if s < n_down:
            b = lax.ppermute(b.astype(wire_dtype), axis, down).astype(jnp.float32)
            if s < n_down - 1:
                b = b + block(me - n_down + 1 + s)
    return block(me) + a + b


def col_reduce_scatter(blocks, n_x, n_y):
    n_col = 2 * n_x * n_y
    c = lax.axis_index("col")
    core = c % 2
    x = (c // 2) % n_x
    y = c // (2 * n_x)
    m = blocks.shape[1] // 2
    halves = blocks.reshape((n_y * n_x, 2, m) + blocks.shape[2:]).astype(jnp.float32)
    keep = lax.dynamic_index_in_dim(halves, core, 1, keepdims=False)
    give = lax.dynamic_index_in_dim(halves, 1 - core, 1, keepdims=False)
    pair = [(j, j ^ 1) for j in range(n_col)]
    summed = keep + lax.ppermute(give, "col", pair)

    def idx(yy, xx, cc):
        return (yy * n_x + xx) * 2 + cc

    def ring(step, size, coord):
        pairs = []
        for yy in range(n_y):
            for xx in range(n_x):
                for cc in range(2):
                    if coord == "x":
                        pairs.append((idx(yy, xx, cc), idx(yy, (xx + step) % size, cc)))
                    else:
                        pairs.append((idx(yy, xx, cc), idx((yy + step) % size, xx, cc)))
        return pairs

    by_x = jnp.swapaxes(summed.reshape((n_y, n_x, m) + blocks.shape[2:]), 0, 1)
    over_x = ring_reduce_scatter(
        by_x, "col", n_x, jnp.bfloat16, me=x, up=ring(1, n_x, "x"), down=ring(-1, n_x, "x")
    )
    return ring_reduce_scatter(
        over_x, "col", n_y, jnp.bfloat16, me=y, up=ring(1, n_y, "y"), down=ring(-1, n_y, "y")
    )


def gather_col(x, n_col):
    spread = jnp.broadcast_to(x[None], (n_col,) + x.shape)
    return lax.all_to_all(spread, "col", 0, 0).reshape((n_col * x.shape[0],) + x.shape[1:])


def shards(inputs, gate_pre, up_pre, w_gate, w_up, w_down, grad_out, n_row, n_col):
    tokens_row, hidden_units = gate_pre.shape
    tokens_col, width = grad_out.shape
    all_pre = lax.all_gather(jnp.stack([gate_pre, up_pre]), "row", axis=1, tiled=True)
    all_grad_out = gather_col(grad_out, n_col)
    all_inputs = gather_col(inputs, n_col)
    part = contract_cols(all_grad_out, w_down).astype(jnp.bfloat16)
    part = part.reshape((n_row, tokens_row, hidden_units))
    own_grad = ring_reduce_scatter(part, "row", n_row, jnp.bfloat16).astype(jnp.bfloat16)
    hidden_grad = ring_all_gather(own_grad[None], "row", n_row).reshape(
        (n_row * tokens_row, hidden_units)
    )
    hidden, gate_grad, up_grad = pointwise(
        all_pre[0], all_pre[1], hidden_grad.astype(jnp.float32)
    )
    grad_down = contract_rows(hidden, all_grad_out).astype(jnp.bfloat16)
    grad_gate = contract_rows(all_inputs, gate_grad).astype(jnp.bfloat16)
    grad_up = contract_rows(all_inputs, up_grad).astype(jnp.bfloat16)
    terms = (
        contract_cols(gate_grad, w_gate) + contract_cols(up_grad, w_up)
    ).astype(jnp.bfloat16)
    received = lax.all_to_all(terms.reshape((n_col, tokens_col, width)), "col", 0, 0)
    grad_in = received.astype(jnp.float32).sum(axis=0).astype(jnp.bfloat16)
    return (grad_in, grad_gate, grad_up, grad_down)


def solution(mesh):
    n_row = mesh.shape["row"]
    n_col = mesh.shape["col"]

    def body(*args):
        return shards(*args, n_row=n_row, n_col=n_col)

    return jax.shard_map(
        body,
        mesh=mesh,
        in_specs=(
            P("col", "row"),
            P("row", "col"),
            P("row", "col"),
            P("row", "col"),
            P("row", "col"),
            P("col", "row"),
            P("col", "row"),
        ),
        out_specs=(P("col", "row"), P("row", "col"), P("row", "col"), P("col", "row")),
        check_vma=False,
    )
```

```python
import jax
import jax.numpy as jnp
from jax import lax
from jax.sharding import PartitionSpec as P


def contract_rows(left, right):
    return lax.dot_general(
        left, right, (((0,), (0,)), ((), ())), preferred_element_type=jnp.float32
    )


def contract_cols(left, right):
    return lax.dot_general(
        left, right, (((1,), (1,)), ((), ())), preferred_element_type=jnp.float32
    )


def pointwise(gate_pre, up_pre, hidden_grad):
    gate_value = gate_pre.astype(jnp.float32)
    up_value = up_pre.astype(jnp.float32)
    sigmoid_gate = jax.nn.sigmoid(gate_value)
    activated = gate_value * sigmoid_gate
    hidden = (activated * up_value).astype(jnp.bfloat16)
    up_grad = (hidden_grad * activated).astype(jnp.bfloat16)
    gate_grad = (
        hidden_grad * up_value * sigmoid_gate * (1.0 + gate_value * (1.0 - sigmoid_gate))
    ).astype(jnp.bfloat16)
    return (hidden, gate_grad, up_grad)


def _shifts(n):
    up = [(j, (j + 1) % n) for j in range(n)]
    down = [(j, (j - 1) % n) for j in range(n)]
    return up, down


def ring_all_gather(x, axis, n):
    me = lax.axis_index(axis)
    up, down = _shifts(n)
    n_up = n // 2
    n_down = n - 1 - n_up
    held = {0: x}
    a = x
    b = x
    for s in range(1, n_up + 1):
        a = lax.ppermute(a, axis, up)
        held[-s] = a
        if s <= n_down:
            b = lax.ppermute(b, axis, down)
            held[s] = b
    ring_order = jnp.stack([held[d] for d in range(-n_up, n_down + 1)], axis=1)
    return jnp.take(ring_order, (jnp.arange(n) - me + n_up) % n, axis=1)


def ring_reduce_scatter(parts, axis, n, wire_dtype, me=None, up=None, down=None):
    if me is None:
        me = lax.axis_index(axis)
        up, down = _shifts(n)
    n_up = n // 2
    n_down = n - 1 - n_up

    def block(j):
        return lax.dynamic_index_in_dim(parts, (j + 2 * n) % n, 0, keepdims=False).astype(
            jnp.float32
        )

    a = block(me + n_up)
    b = block(me - n_down)
    for s in range(n_up):
        a = lax.ppermute(a.astype(wire_dtype), axis, up).astype(jnp.float32)
        if s < n_up - 1:
            a = a + block(me + n_up - 1 - s)
        if s < n_down:
            b = lax.ppermute(b.astype(wire_dtype), axis, down).astype(jnp.float32)
            if s < n_down - 1:
                b = b + block(me - n_down + 1 + s)
    return block(me) + a + b


def col_reduce_scatter(blocks, n_x, n_y):
    n_col = 2 * n_x * n_y
    c = lax.axis_index("col")
    core = c % 2
    x = (c // 2) % n_x
    y = c // (2 * n_x)
    m = blocks.shape[1] // 2
    halves = blocks.reshape((n_y * n_x, 2, m) + blocks.shape[2:]).astype(jnp.float32)
    keep = lax.dynamic_index_in_dim(halves, core, 1, keepdims=False)
    give = lax.dynamic_index_in_dim(halves, 1 - core, 1, keepdims=False)
    pair = [(j, j ^ 1) for j in range(n_col)]
    summed = keep + lax.ppermute(give, "col", pair)

    def idx(yy, xx, cc):
        return (yy * n_x + xx) * 2 + cc

    def ring(step, size, coord):
        pairs = []
        for yy in range(n_y):
            for xx in range(n_x):
                for cc in range(2):
                    if coord == "x":
                        pairs.append((idx(yy, xx, cc), idx(yy, (xx + step) % size, cc)))
                    else:
                        pairs.append((idx(yy, xx, cc), idx((yy + step) % size, xx, cc)))
        return pairs

    by_x = jnp.swapaxes(summed.reshape((n_y, n_x, m) + blocks.shape[2:]), 0, 1)
    over_x = ring_reduce_scatter(
        by_x, "col", n_x, jnp.bfloat16, me=x, up=ring(1, n_x, "x"), down=ring(-1, n_x, "x")
    )
    return ring_reduce_scatter(
        over_x, "col", n_y, jnp.bfloat16, me=y, up=ring(1, n_y, "y"), down=ring(-1, n_y, "y")
    )


def gather_col(x, n_col):
    spread = jnp.broadcast_to(x[None], (n_col,) + x.shape)
    return lax.all_to_all(spread, "col", 0, 0).reshape((n_col * x.shape[0],) + x.shape[1:])


def shards(inputs, gate_pre, up_pre, w_gate, w_up, w_down, grad_out, n_row, n_col):
    tokens_row, hidden_units = gate_pre.shape
    tokens_col, width = grad_out.shape
    half = width // 2
    out_a = gather_col(grad_out[:, :half], n_col)
    out_b = lax.all_gather(grad_out[:, half:], "col", axis=0, tiled=True)
    all_pre = lax.all_gather(jnp.stack([gate_pre, up_pre]), "row", axis=1, tiled=True)
    all_inputs = lax.all_gather(inputs, "col", axis=0, tiled=True)
    part = (
        contract_cols(out_a, w_down[:, :half]) + contract_cols(out_b, w_down[:, half:])
    ).astype(jnp.bfloat16)
    all_grad_out = jnp.concatenate([out_a, out_b], axis=1)
    part = part.reshape((n_row, tokens_row, hidden_units))
    own_grad = ring_reduce_scatter(part, "row", n_row, jnp.bfloat16).astype(jnp.bfloat16)
    hidden_grad = ring_all_gather(own_grad[None], "row", n_row).reshape(
        (n_row * tokens_row, hidden_units)
    )
    hidden, gate_grad, up_grad = pointwise(
        all_pre[0], all_pre[1], hidden_grad.astype(jnp.float32)
    )
    grad_down = contract_rows(hidden, all_grad_out).astype(jnp.bfloat16)
    grad_gate = contract_rows(all_inputs, gate_grad).astype(jnp.bfloat16)
    grad_up = contract_rows(all_inputs, up_grad).astype(jnp.bfloat16)
    terms = (
        contract_cols(gate_grad, w_gate) + contract_cols(up_grad, w_up)
    ).astype(jnp.bfloat16)
    received = lax.all_to_all(terms.reshape((n_col, tokens_col, width)), "col", 0, 0)
    grad_in = received.astype(jnp.float32).sum(axis=0).astype(jnp.bfloat16)
    return (grad_in, grad_gate, grad_up, grad_down)


def solution(mesh):
    n_row = mesh.shape["row"]
    n_col = mesh.shape["col"]

    def body(*args):
        return shards(*args, n_row=n_row, n_col=n_col)

    return jax.shard_map(
        body,
        mesh=mesh,
        in_specs=(
            P("col", "row"),
            P("row", "col"),
            P("row", "col"),
            P("row", "col"),
            P("row", "col"),
            P("col", "row"),
            P("col", "row"),
        ),
        out_specs=(P("col", "row"), P("row", "col"), P("row", "col"), P("col", "row")),
        check_vma=False,
    )
```

```python
import jax
import jax.numpy as jnp
from jax import lax
from jax.sharding import PartitionSpec as P


def contract_rows(left, right):
    return lax.dot_general(
        left, right, (((0,), (0,)), ((), ())), preferred_element_type=jnp.float32
    )


def contract_cols(left, right):
    return lax.dot_general(
        left, right, (((1,), (1,)), ((), ())), preferred_element_type=jnp.float32
    )


def pointwise(gate_pre, up_pre, hidden_grad):
    gate_value = gate_pre.astype(jnp.float32)
    up_value = up_pre.astype(jnp.float32)
    sigmoid_gate = jax.nn.sigmoid(gate_value)
    activated = gate_value * sigmoid_gate
    hidden = (activated * up_value).astype(jnp.bfloat16)
    up_grad = (hidden_grad * activated).astype(jnp.bfloat16)
    gate_grad = (
        hidden_grad * up_value * sigmoid_gate * (1.0 + gate_value * (1.0 - sigmoid_gate))
    ).astype(jnp.bfloat16)
    return (hidden, gate_grad, up_grad)


def _shifts(n):
    up = [(j, (j + 1) % n) for j in range(n)]
    down = [(j, (j - 1) % n) for j in range(n)]
    return up, down


def ring_all_gather(x, axis, n):
    me = lax.axis_index(axis)
    up, down = _shifts(n)
    n_up = n // 2
    n_down = n - 1 - n_up
    held = {0: x}
    a = x
    b = x
    for s in range(1, n_up + 1):
        a = lax.ppermute(a, axis, up)
        held[-s] = a
        if s <= n_down:
            b = lax.ppermute(b, axis, down)
            held[s] = b
    ring_order = jnp.stack([held[d] for d in range(-n_up, n_down + 1)], axis=1)
    return jnp.take(ring_order, (jnp.arange(n) - me + n_up) % n, axis=1)


def ring_reduce_scatter(parts, axis, n, wire_dtype, me=None, up=None, down=None):
    if me is None:
        me = lax.axis_index(axis)
        up, down = _shifts(n)
    n_up = n // 2
    n_down = n - 1 - n_up

    def block(j):
        return lax.dynamic_index_in_dim(parts, (j + 2 * n) % n, 0, keepdims=False).astype(
            jnp.float32
        )

    a = block(me + n_up)
    b = block(me - n_down)
    for s in range(n_up):
        a = lax.ppermute(a.astype(wire_dtype), axis, up).astype(jnp.float32)
        if s < n_up - 1:
            a = a + block(me + n_up - 1 - s)
        if s < n_down:
            b = lax.ppermute(b.astype(wire_dtype), axis, down).astype(jnp.float32)
            if s < n_down - 1:
                b = b + block(me - n_down + 1 + s)
    return block(me) + a + b


def col_reduce_scatter(blocks, n_x, n_y):
    n_col = 2 * n_x * n_y
    c = lax.axis_index("col")
    core = c % 2
    x = (c // 2) % n_x
    y = c // (2 * n_x)
    m = blocks.shape[1] // 2
    halves = blocks.reshape((n_y * n_x, 2, m) + blocks.shape[2:]).astype(jnp.float32)
    keep = lax.dynamic_index_in_dim(halves, core, 1, keepdims=False)
    give = lax.dynamic_index_in_dim(halves, 1 - core, 1, keepdims=False)
    pair = [(j, j ^ 1) for j in range(n_col)]
    summed = keep + lax.ppermute(give, "col", pair)

    def idx(yy, xx, cc):
        return (yy * n_x + xx) * 2 + cc

    def ring(step, size, coord):
        pairs = []
        for yy in range(n_y):
            for xx in range(n_x):
                for cc in range(2):
                    if coord == "x":
                        pairs.append((idx(yy, xx, cc), idx(yy, (xx + step) % size, cc)))
                    else:
                        pairs.append((idx(yy, xx, cc), idx((yy + step) % size, xx, cc)))
        return pairs

    by_x = jnp.swapaxes(summed.reshape((n_y, n_x, m) + blocks.shape[2:]), 0, 1)
    over_x = ring_reduce_scatter(
        by_x, "col", n_x, jnp.bfloat16, me=x, up=ring(1, n_x, "x"), down=ring(-1, n_x, "x")
    )
    return ring_reduce_scatter(
        over_x, "col", n_y, jnp.bfloat16, me=y, up=ring(1, n_y, "y"), down=ring(-1, n_y, "y")
    )


def gather_col(x, n_col):
    core = lax.axis_index("col") % 2
    other = lax.ppermute(x, "col", [(j, j ^ 1) for j in range(n_col)])
    chip = jnp.where(core == 0, jnp.concatenate([x, other]), jnp.concatenate([other, x]))
    groups = [[j for j in range(n_col) if j % 2 == k] for k in (0, 1)]
    spread = jnp.broadcast_to(chip[None], (n_col // 2,) + chip.shape)
    gathered = lax.all_to_all(spread, "col", 0, 0, axis_index_groups=groups)
    return gathered.reshape((n_col * x.shape[0],) + x.shape[1:])


def shards(inputs, gate_pre, up_pre, w_gate, w_up, w_down, grad_out, n_row, n_col):
    tokens_row, hidden_units = gate_pre.shape
    tokens_col, width = grad_out.shape
    all_pre = lax.all_gather(jnp.stack([gate_pre, up_pre]), "row", axis=1, tiled=True)
    all_grad_out = gather_col(grad_out, n_col)
    all_inputs = lax.all_gather(inputs, "col", axis=0, tiled=True)
    part = contract_cols(all_grad_out, w_down).astype(jnp.bfloat16)
    part = part.reshape((n_row, tokens_row, hidden_units))
    own_grad = ring_reduce_scatter(part, "row", n_row, jnp.bfloat16).astype(jnp.bfloat16)
    hidden_grad = ring_all_gather(own_grad[None], "row", n_row).reshape(
        (n_row * tokens_row, hidden_units)
    )
    hidden, gate_grad, up_grad = pointwise(
        all_pre[0], all_pre[1], hidden_grad.astype(jnp.float32)
    )
    grad_down = contract_rows(hidden, all_grad_out).astype(jnp.bfloat16)
    grad_gate = contract_rows(all_inputs, gate_grad).astype(jnp.bfloat16)
    grad_up = contract_rows(all_inputs, up_grad).astype(jnp.bfloat16)
    terms = (
        contract_cols(gate_grad, w_gate) + contract_cols(up_grad, w_up)
    ).astype(jnp.bfloat16)
    received = lax.all_to_all(terms.reshape((n_col, tokens_col, width)), "col", 0, 0)
    grad_in = received.astype(jnp.float32).sum(axis=0).astype(jnp.bfloat16)
    return (grad_in, grad_gate, grad_up, grad_down)


def solution(mesh):
    n_row = mesh.shape["row"]
    n_col = mesh.shape["col"]

    def body(*args):
        return shards(*args, n_row=n_row, n_col=n_col)

    return jax.shard_map(
        body,
        mesh=mesh,
        in_specs=(
            P("col", "row"),
            P("row", "col"),
            P("row", "col"),
            P("row", "col"),
            P("row", "col"),
            P("col", "row"),
            P("col", "row"),
        ),
        out_specs=(P("col", "row"), P("row", "col"), P("row", "col"), P("col", "row")),
        check_vma=False,
    )
```

```python
import jax
import jax.numpy as jnp
from jax import lax
from jax.sharding import PartitionSpec as P


def contract_rows(left, right):
    return lax.dot_general(
        left, right, (((0,), (0,)), ((), ())), preferred_element_type=jnp.float32
    )


def contract_cols(left, right):
    return lax.dot_general(
        left, right, (((1,), (1,)), ((), ())), preferred_element_type=jnp.float32
    )


def pointwise(gate_pre, up_pre, hidden_grad):
    gate_value = gate_pre.astype(jnp.float32)
    up_value = up_pre.astype(jnp.float32)
    sigmoid_gate = jax.nn.sigmoid(gate_value)
    activated = gate_value * sigmoid_gate
    hidden = (activated * up_value).astype(jnp.bfloat16)
    up_grad = (hidden_grad * activated).astype(jnp.bfloat16)
    gate_grad = (
        hidden_grad * up_value * sigmoid_gate * (1.0 + gate_value * (1.0 - sigmoid_gate))
    ).astype(jnp.bfloat16)
    return (hidden, gate_grad, up_grad)


def _shifts(n):
    up = [(j, (j + 1) % n) for j in range(n)]
    down = [(j, (j - 1) % n) for j in range(n)]
    return up, down


def ring_all_gather(x, axis, n):
    me = lax.axis_index(axis)
    up, down = _shifts(n)
    n_up = n // 2
    n_down = n - 1 - n_up
    held = {0: x}
    a = x
    b = x
    for s in range(1, n_up + 1):
        a = lax.ppermute(a, axis, up)
        held[-s] = a
        if s <= n_down:
            b = lax.ppermute(b, axis, down)
            held[s] = b
    ring_order = jnp.stack([held[d] for d in range(-n_up, n_down + 1)], axis=1)
    return jnp.take(ring_order, (jnp.arange(n) - me + n_up) % n, axis=1)


def ring_reduce_scatter(parts, axis, n, wire_dtype, me=None, up=None, down=None):
    if me is None:
        me = lax.axis_index(axis)
        up, down = _shifts(n)
    n_up = n // 2
    n_down = n - 1 - n_up

    def block(j):
        return lax.dynamic_index_in_dim(parts, (j + 2 * n) % n, 0, keepdims=False).astype(
            jnp.float32
        )

    a = block(me + n_up)
    b = block(me - n_down)
    for s in range(n_up):
        a = lax.ppermute(a.astype(wire_dtype), axis, up).astype(jnp.float32)
        if s < n_up - 1:
            a = a + block(me + n_up - 1 - s)
        if s < n_down:
            b = lax.ppermute(b.astype(wire_dtype), axis, down).astype(jnp.float32)
            if s < n_down - 1:
                b = b + block(me - n_down + 1 + s)
    return block(me) + a + b


def col_reduce_scatter(blocks, n_x, n_y):
    n_col = 2 * n_x * n_y
    c = lax.axis_index("col")
    core = c % 2
    x = (c // 2) % n_x
    y = c // (2 * n_x)
    m = blocks.shape[1] // 2
    halves = blocks.reshape((n_y * n_x, 2, m) + blocks.shape[2:]).astype(jnp.float32)
    keep = lax.dynamic_index_in_dim(halves, core, 1, keepdims=False)
    give = lax.dynamic_index_in_dim(halves, 1 - core, 1, keepdims=False)
    pair = [(j, j ^ 1) for j in range(n_col)]
    summed = keep + lax.ppermute(give, "col", pair)

    def idx(yy, xx, cc):
        return (yy * n_x + xx) * 2 + cc

    def ring(step, size, coord):
        pairs = []
        for yy in range(n_y):
            for xx in range(n_x):
                for cc in range(2):
                    if coord == "x":
                        pairs.append((idx(yy, xx, cc), idx(yy, (xx + step) % size, cc)))
                    else:
                        pairs.append((idx(yy, xx, cc), idx((yy + step) % size, xx, cc)))
        return pairs

    by_x = jnp.swapaxes(summed.reshape((n_y, n_x, m) + blocks.shape[2:]), 0, 1)
    over_x = ring_reduce_scatter(
        by_x, "col", n_x, jnp.bfloat16, me=x, up=ring(1, n_x, "x"), down=ring(-1, n_x, "x")
    )
    return ring_reduce_scatter(
        over_x, "col", n_y, jnp.bfloat16, me=y, up=ring(1, n_y, "y"), down=ring(-1, n_y, "y")
    )


def gather_col_flat(x, n_col):
    spread = jnp.broadcast_to(x[None], (n_col,) + x.shape)
    return lax.all_to_all(spread, "col", 0, 0).reshape((n_col * x.shape[0],) + x.shape[1:])


def gather_col(x, n_col):
    core = lax.axis_index("col") % 2
    other = lax.ppermute(x, "col", [(j, j ^ 1) for j in range(n_col)])
    chip = jnp.where(core == 0, jnp.concatenate([x, other]), jnp.concatenate([other, x]))
    groups = [[j for j in range(n_col) if j % 2 == k] for k in (0, 1)]
    spread = jnp.broadcast_to(chip[None], (n_col // 2,) + chip.shape)
    gathered = lax.all_to_all(spread, "col", 0, 0, axis_index_groups=groups)
    return gathered.reshape((n_col * x.shape[0],) + x.shape[1:])


def shards(inputs, gate_pre, up_pre, w_gate, w_up, w_down, grad_out, n_row, n_col):
    tokens_row, hidden_units = gate_pre.shape
    tokens_col, width = grad_out.shape
    all_pre = lax.all_gather(jnp.stack([gate_pre, up_pre]), "row", axis=1, tiled=True)
    all_grad_out = gather_col_flat(grad_out, n_col)
    all_inputs = lax.all_gather(inputs, "col", axis=0, tiled=True)
    part = contract_cols(all_grad_out, w_down).astype(jnp.bfloat16)
    part = part.reshape((n_row, tokens_row, hidden_units))
    own_grad = ring_reduce_scatter(part, "row", n_row, jnp.bfloat16).astype(jnp.bfloat16)
    hidden_grad = ring_all_gather(own_grad[None], "row", n_row).reshape(
        (n_row * tokens_row, hidden_units)
    )
    hidden, gate_grad, up_grad = pointwise(
        all_pre[0], all_pre[1], hidden_grad.astype(jnp.float32)
    )
    grad_down = contract_rows(hidden, all_grad_out).astype(jnp.bfloat16)
    terms = (
        contract_cols(gate_grad, w_gate) + contract_cols(up_grad, w_up)
    ).astype(jnp.bfloat16)
    received = lax.all_to_all(terms.reshape((n_col, tokens_col, width)), "col", 0, 0)
    received, all_inputs = lax.optimization_barrier((received, all_inputs))
    grad_gate = contract_rows(all_inputs, gate_grad).astype(jnp.bfloat16)
    grad_up = contract_rows(all_inputs, up_grad).astype(jnp.bfloat16)
    grad_in = received.astype(jnp.float32).sum(axis=0).astype(jnp.bfloat16)
    return (grad_in, grad_gate, grad_up, grad_down)


def solution(mesh):
    n_row = mesh.shape["row"]
    n_col = mesh.shape["col"]

    def body(*args):
        return shards(*args, n_row=n_row, n_col=n_col)

    return jax.shard_map(
        body,
        mesh=mesh,
        in_specs=(
            P("col", "row"),
            P("row", "col"),
            P("row", "col"),
            P("row", "col"),
            P("row", "col"),
            P("col", "row"),
            P("col", "row"),
        ),
        out_specs=(P("col", "row"), P("row", "col"), P("row", "col"), P("col", "row")),
        check_vma=False,
    )
```

```python
import jax
import jax.numpy as jnp
from jax import lax
from jax.sharding import PartitionSpec as P


def contract_rows(left, right):
    return lax.dot_general(
        left, right, (((0,), (0,)), ((), ())), preferred_element_type=jnp.float32
    )


def contract_cols(left, right):
    return lax.dot_general(
        left, right, (((1,), (1,)), ((), ())), preferred_element_type=jnp.float32
    )


def pointwise(gate_pre, up_pre, hidden_grad):
    gate_value = gate_pre.astype(jnp.float32)
    up_value = up_pre.astype(jnp.float32)
    sigmoid_gate = jax.nn.sigmoid(gate_value)
    activated = gate_value * sigmoid_gate
    hidden = (activated * up_value).astype(jnp.bfloat16)
    up_grad = (hidden_grad * activated).astype(jnp.bfloat16)
    gate_grad = (
        hidden_grad * up_value * sigmoid_gate * (1.0 + gate_value * (1.0 - sigmoid_gate))
    ).astype(jnp.bfloat16)
    return (hidden, gate_grad, up_grad)


def _shifts(n):
    up = [(j, (j + 1) % n) for j in range(n)]
    down = [(j, (j - 1) % n) for j in range(n)]
    return up, down


def ring_all_gather(x, axis, n):
    me = lax.axis_index(axis)
    up, down = _shifts(n)
    n_up = n // 2
    n_down = n - 1 - n_up
    held = {0: x}
    a = x
    b = x
    for s in range(1, n_up + 1):
        a = lax.ppermute(a, axis, up)
        held[-s] = a
        if s <= n_down:
            b = lax.ppermute(b, axis, down)
            held[s] = b
    ring_order = jnp.stack([held[d] for d in range(-n_up, n_down + 1)], axis=1)
    return jnp.take(ring_order, (jnp.arange(n) - me + n_up) % n, axis=1)


def ring_reduce_scatter(parts, axis, n, wire_dtype, me=None, up=None, down=None):
    if me is None:
        me = lax.axis_index(axis)
        up, down = _shifts(n)
    n_up = n // 2
    n_down = n - 1 - n_up

    def block(j):
        return lax.dynamic_index_in_dim(parts, (j + 2 * n) % n, 0, keepdims=False).astype(
            jnp.float32
        )

    a = block(me + n_up)
    b = block(me - n_down)
    for s in range(n_up):
        a = lax.ppermute(a.astype(wire_dtype), axis, up).astype(jnp.float32)
        if s < n_up - 1:
            a = a + block(me + n_up - 1 - s)
        if s < n_down:
            b = lax.ppermute(b.astype(wire_dtype), axis, down).astype(jnp.float32)
            if s < n_down - 1:
                b = b + block(me - n_down + 1 + s)
    return block(me) + a + b


def col_reduce_scatter(blocks, n_x, n_y):
    n_col = 2 * n_x * n_y
    c = lax.axis_index("col")
    core = c % 2
    x = (c // 2) % n_x
    y = c // (2 * n_x)
    m = blocks.shape[1] // 2
    halves = blocks.reshape((n_y * n_x, 2, m) + blocks.shape[2:]).astype(jnp.float32)
    keep = lax.dynamic_index_in_dim(halves, core, 1, keepdims=False)
    give = lax.dynamic_index_in_dim(halves, 1 - core, 1, keepdims=False)
    pair = [(j, j ^ 1) for j in range(n_col)]
    summed = keep + lax.ppermute(give, "col", pair)

    def idx(yy, xx, cc):
        return (yy * n_x + xx) * 2 + cc

    def ring(step, size, coord):
        pairs = []
        for yy in range(n_y):
            for xx in range(n_x):
                for cc in range(2):
                    if coord == "x":
                        pairs.append((idx(yy, xx, cc), idx(yy, (xx + step) % size, cc)))
                    else:
                        pairs.append((idx(yy, xx, cc), idx((yy + step) % size, xx, cc)))
        return pairs

    by_x = jnp.swapaxes(summed.reshape((n_y, n_x, m) + blocks.shape[2:]), 0, 1)
    over_x = ring_reduce_scatter(
        by_x, "col", n_x, jnp.bfloat16, me=x, up=ring(1, n_x, "x"), down=ring(-1, n_x, "x")
    )
    return ring_reduce_scatter(
        over_x, "col", n_y, jnp.bfloat16, me=y, up=ring(1, n_y, "y"), down=ring(-1, n_y, "y")
    )


def gather_col_flat(x, n_col):
    spread = jnp.broadcast_to(x[None], (n_col,) + x.shape)
    return lax.all_to_all(spread, "col", 0, 0).reshape((n_col * x.shape[0],) + x.shape[1:])


def gather_col(x, n_col):
    core = lax.axis_index("col") % 2
    other = lax.ppermute(x, "col", [(j, j ^ 1) for j in range(n_col)])
    chip = jnp.where(core == 0, jnp.concatenate([x, other]), jnp.concatenate([other, x]))
    groups = [[j for j in range(n_col) if j % 2 == k] for k in (0, 1)]
    spread = jnp.broadcast_to(chip[None], (n_col // 2,) + chip.shape)
    gathered = lax.all_to_all(spread, "col", 0, 0, axis_index_groups=groups)
    return gathered.reshape((n_col * x.shape[0],) + x.shape[1:])


def shards(inputs, gate_pre, up_pre, w_gate, w_up, w_down, grad_out, n_row, n_col):
    tokens_row, hidden_units = gate_pre.shape
    tokens_col, width = grad_out.shape
    all_pre = lax.all_gather(jnp.stack([gate_pre, up_pre]), "row", axis=1, tiled=True)
    all_grad_out = gather_col_flat(grad_out, n_col)
    all_inputs = lax.all_gather(inputs, "col", axis=0, tiled=True)
    part = contract_cols(all_grad_out, w_down).astype(jnp.bfloat16)
    part = part.reshape((n_row, tokens_row, hidden_units))
    own_grad = ring_reduce_scatter(part, "row", n_row, jnp.bfloat16).astype(jnp.bfloat16)
    own_grad, all_inputs = lax.optimization_barrier((own_grad, all_inputs))
    hidden_grad = ring_all_gather(own_grad[None], "row", n_row).reshape(
        (n_row * tokens_row, hidden_units)
    )
    hidden, gate_grad, up_grad = pointwise(
        all_pre[0], all_pre[1], hidden_grad.astype(jnp.float32)
    )
    grad_down = contract_rows(hidden, all_grad_out).astype(jnp.bfloat16)
    terms = (
        contract_cols(gate_grad, w_gate) + contract_cols(up_grad, w_up)
    ).astype(jnp.bfloat16)
    received = lax.all_to_all(terms.reshape((n_col, tokens_col, width)), "col", 0, 0)
    received, all_inputs = lax.optimization_barrier((received, all_inputs))
    grad_gate = contract_rows(all_inputs, gate_grad).astype(jnp.bfloat16)
    grad_up = contract_rows(all_inputs, up_grad).astype(jnp.bfloat16)
    grad_in = received.astype(jnp.float32).sum(axis=0).astype(jnp.bfloat16)
    return (grad_in, grad_gate, grad_up, grad_down)


def solution(mesh):
    n_row = mesh.shape["row"]
    n_col = mesh.shape["col"]

    def body(*args):
        return shards(*args, n_row=n_row, n_col=n_col)

    return jax.shard_map(
        body,
        mesh=mesh,
        in_specs=(
            P("col", "row"),
            P("row", "col"),
            P("row", "col"),
            P("row", "col"),
            P("row", "col"),
            P("col", "row"),
            P("col", "row"),
        ),
        out_specs=(P("col", "row"), P("row", "col"), P("row", "col"), P("col", "row")),
        check_vma=False,
    )
```

```python
import jax
import jax.numpy as jnp
from jax import lax
from jax.sharding import PartitionSpec as P


def contract_rows(left, right):
    return lax.dot_general(
        left, right, (((0,), (0,)), ((), ())), preferred_element_type=jnp.float32
    )


def contract_cols(left, right):
    return lax.dot_general(
        left, right, (((1,), (1,)), ((), ())), preferred_element_type=jnp.float32
    )


def pointwise(gate_pre, up_pre, hidden_grad):
    gate_value = gate_pre.astype(jnp.float32)
    up_value = up_pre.astype(jnp.float32)
    sigmoid_gate = jax.nn.sigmoid(gate_value)
    activated = gate_value * sigmoid_gate
    hidden = (activated * up_value).astype(jnp.bfloat16)
    up_grad = (hidden_grad * activated).astype(jnp.bfloat16)
    gate_grad = (
        hidden_grad * up_value * sigmoid_gate * (1.0 + gate_value * (1.0 - sigmoid_gate))
    ).astype(jnp.bfloat16)
    return (hidden, gate_grad, up_grad)


def _shifts(n):
    up = [(j, (j + 1) % n) for j in range(n)]
    down = [(j, (j - 1) % n) for j in range(n)]
    return up, down


def ring_all_gather(x, axis, n):
    me = lax.axis_index(axis)
    up, down = _shifts(n)
    n_up = n // 2
    n_down = n - 1 - n_up
    held = {0: x}
    a = x
    b = x
    for s in range(1, n_up + 1):
        a = lax.ppermute(a, axis, up)
        held[-s] = a
        if s <= n_down:
            b = lax.ppermute(b, axis, down)
            held[s] = b
    ring_order = jnp.stack([held[d] for d in range(-n_up, n_down + 1)], axis=1)
    return jnp.take(ring_order, (jnp.arange(n) - me + n_up) % n, axis=1)


def ring_reduce_scatter(parts, axis, n, wire_dtype, me=None, up=None, down=None):
    if me is None:
        me = lax.axis_index(axis)
        up, down = _shifts(n)
    n_up = n // 2
    n_down = n - 1 - n_up

    def block(j):
        return lax.dynamic_index_in_dim(parts, (j + 2 * n) % n, 0, keepdims=False).astype(
            jnp.float32
        )

    a = block(me + n_up)
    b = block(me - n_down)
    for s in range(n_up):
        a = lax.ppermute(a.astype(wire_dtype), axis, up).astype(jnp.float32)
        if s < n_up - 1:
            a = a + block(me + n_up - 1 - s)
        if s < n_down:
            b = lax.ppermute(b.astype(wire_dtype), axis, down).astype(jnp.float32)
            if s < n_down - 1:
                b = b + block(me - n_down + 1 + s)
    return block(me) + a + b


def col_reduce_scatter(blocks, n_x, n_y):
    n_col = 2 * n_x * n_y
    c = lax.axis_index("col")
    core = c % 2
    x = (c // 2) % n_x
    y = c // (2 * n_x)
    m = blocks.shape[1] // 2
    halves = blocks.reshape((n_y * n_x, 2, m) + blocks.shape[2:]).astype(jnp.float32)
    keep = lax.dynamic_index_in_dim(halves, core, 1, keepdims=False)
    give = lax.dynamic_index_in_dim(halves, 1 - core, 1, keepdims=False)
    pair = [(j, j ^ 1) for j in range(n_col)]
    summed = keep + lax.ppermute(give, "col", pair)

    def idx(yy, xx, cc):
        return (yy * n_x + xx) * 2 + cc

    def ring(step, size, coord):
        pairs = []
        for yy in range(n_y):
            for xx in range(n_x):
                for cc in range(2):
                    if coord == "x":
                        pairs.append((idx(yy, xx, cc), idx(yy, (xx + step) % size, cc)))
                    else:
                        pairs.append((idx(yy, xx, cc), idx((yy + step) % size, xx, cc)))
        return pairs

    by_x = jnp.swapaxes(summed.reshape((n_y, n_x, m) + blocks.shape[2:]), 0, 1)
    over_x = ring_reduce_scatter(
        by_x, "col", n_x, jnp.bfloat16, me=x, up=ring(1, n_x, "x"), down=ring(-1, n_x, "x")
    )
    return ring_reduce_scatter(
        over_x, "col", n_y, jnp.bfloat16, me=y, up=ring(1, n_y, "y"), down=ring(-1, n_y, "y")
    )


def gather_col_flat(x, n_col):
    spread = jnp.broadcast_to(x[None], (n_col,) + x.shape)
    return lax.all_to_all(spread, "col", 0, 0).reshape((n_col * x.shape[0],) + x.shape[1:])


def gather_col(x, n_col):
    core = lax.axis_index("col") % 2
    other = lax.ppermute(x, "col", [(j, j ^ 1) for j in range(n_col)])
    chip = jnp.where(core == 0, jnp.concatenate([x, other]), jnp.concatenate([other, x]))
    groups = [[j for j in range(n_col) if j % 2 == k] for k in (0, 1)]
    spread = jnp.broadcast_to(chip[None], (n_col // 2,) + chip.shape)
    gathered = lax.all_to_all(spread, "col", 0, 0, axis_index_groups=groups)
    return gathered.reshape((n_col * x.shape[0],) + x.shape[1:])


def shards(inputs, gate_pre, up_pre, w_gate, w_up, w_down, grad_out, n_row, n_col):
    tokens_row, hidden_units = gate_pre.shape
    tokens_col, width = grad_out.shape
    all_pre = lax.all_gather(jnp.stack([gate_pre, up_pre]), "row", axis=1, tiled=True)
    all_grad_out = gather_col_flat(grad_out, n_col)
    all_inputs = lax.all_gather(inputs, "col", axis=0, tiled=True)
    part = contract_cols(all_grad_out, w_down).astype(jnp.bfloat16)
    part = part.reshape((n_row, tokens_row, hidden_units))
    own_grad = ring_reduce_scatter(part, "row", n_row, jnp.bfloat16).astype(jnp.bfloat16)
    hidden_grad = ring_all_gather(own_grad[None], "row", n_row).reshape(
        (n_row * tokens_row, hidden_units)
    )
    hidden, gate_grad, up_grad = pointwise(
        all_pre[0], all_pre[1], hidden_grad.astype(jnp.float32)
    )
    grad_down = contract_rows(hidden, all_grad_out).astype(jnp.bfloat16)
    grad_gate = contract_rows(all_inputs, gate_grad).astype(jnp.bfloat16)
    grad_up = contract_rows(all_inputs, up_grad).astype(jnp.bfloat16)
    terms = (
        contract_cols(gate_grad, w_gate) + contract_cols(up_grad, w_up)
    ).astype(jnp.bfloat16)
    received = lax.all_to_all(terms.reshape((n_col, tokens_col, width)), "col", 0, 0)
    grad_in = received.astype(jnp.float32).sum(axis=0).astype(jnp.bfloat16)
    return (grad_in, grad_gate, grad_up, grad_down)


def solution(mesh):
    n_row = mesh.shape["row"]
    n_col = mesh.shape["col"]

    def body(*args):
        return shards(*args, n_row=n_row, n_col=n_col)

    return jax.shard_map(
        body,
        mesh=mesh,
        in_specs=(
            P("col", "row"),
            P("row", "col"),
            P("row", "col"),
            P("row", "col"),
            P("row", "col"),
            P("col", "row"),
            P("col", "row"),
        ),
        out_specs=(P("col", "row"), P("row", "col"), P("row", "col"), P("col", "row")),
        check_vma=False,
    )
```
